512 devices in a mesh: ctx: 64 (over z, y), tp: 8 (over x, core).
Axes of the slice: x: 4, y: 4, z: 16, core: 2. Of those that a mesh axis runs over, the one named last changes fastest.
Arguments:
- features: bfloat16 [3, 4096, 8192], P(None, 'ctx', 'tp'), may hold values from -6 to 6
- short_weight: float32 [3, 3, 8192], P(None, None, 'tp'), may hold values from -3 to 3
- decay_rate: float32 [512, 16], P('tp'), may hold values from 0.00012207031 to 0.03
- residue: float32 [512, 16], P('tp'), may hold values from -3 to 3
- skip_gain: float32 [8192], P('tp'), may hold values from -1 to 1
- out_weight: bfloat16 [8192, 4096], P('tp', 'ctx'), may hold values from -0.1875 to 0.1875
Outputs:
- mixed_out: bfloat16 [4096, 4096], P('ctx', 'tp')
The draws below stay inside these ranges and needn't reach their ends.
All inputs are finite; a program needn't handle non-finite values.
Results may differ from the reference program's by a relative error of at most 0.006.
Values may be sent and summed in bfloat16 or wider, within the bound.
No kernel may reach another device: no remote copies, remote signals or barrier semaphores. Data moves between devices by JAX's collectives and lax.ppermute only.
A program may use at most 128 MiB of HBM per device.

```python
import math
import jax
import jax.numpy as jnp
from jax import lax

D = 8192
D_OUT = 4096
G = 512
S = 16
KS = 3
TOK_DEV = 64
SEQ = 4096


def with_spikes(drawn, key, source, target, parts, factor):
    owner, partner = [(jnp.arange(drawn.shape[axis_at]) // (drawn.shape[axis_at] // parts)).reshape([-1 if axis == axis_at else 1 for axis in range(drawn.ndim)]) for axis_at in (source, target)]
    chosen = jax.random.permutation(key, parts)[partner]
    strong = (owner == chosen) | (owner == (partner + parts // 2) % parts)
    return jnp.where(strong, factor * drawn, drawn)


def steps_of(key, dims, cuts, least, largest):
    gain, own = 1.0, jax.random.fold_in(key, 6)
    for axis_at, parts in cuts:
        steps = jnp.exp(jax.random.uniform(jax.random.fold_in(own, axis_at), (parts,), jnp.float32, least / len(cuts), largest / len(cuts)))
        gain = gain * jnp.repeat(steps, dims[axis_at] // parts).reshape([-1 if axis == axis_at else 1 for axis in range(len(dims))])
    return gain


def gaussian(rng, shape, scale, bound, split=(), kind=jnp.bfloat16):
    entries = scale * jax.random.normal(rng, shape, jnp.float32)
    if split:
        entries = entries * steps_of(rng, shape, split, -0.22, 0.18)
    return jnp.clip(entries, -bound, bound).astype(kind)


def bell_draw_with(rng, extent, scale, bound, shards, heavy, held_as=jnp.bfloat16):
    drawn = scale * jax.random.normal(rng, extent, jnp.float32)
    if shards:
        drawn = drawn * steps_of(rng, extent, shards, -0.22, 0.18)
    return jnp.clip(with_spikes(drawn, jax.random.fold_in(rng, 3), *heavy), -bound, bound).astype(held_as)


def setup_inputs(seed: int = 0) -> dict:
    key_of = jax.random.split(jax.random.key(seed), 7)
    features = gaussian(key_of[0], (3, SEQ, D), 1.0, 6.0, ((1, 64), (2, 8)))
    short_weight = gaussian(key_of[1], (3, KS, D), 0.6, 3.0, ((2, 8),), jnp.float32)
    decay_rate = jnp.clip(jnp.exp(math.log(0.03) - 5.5043554 * jax.random.uniform(key_of[2], (G, S), jnp.float32) ** steps_of(key_of[2], (G, S), ((0, 8),), -0.2, 0.2)), 0.00012207031, 0.03)
    residue = gaussian(key_of[3], (G, S), 0.5, 3.0, ((0, 8),), jnp.float32)
    skip_gain = jnp.clip(jax.random.uniform(key_of[4], (D,), jnp.float32, -1.0, 1.0) * steps_of(key_of[4], (D,), ((0, 8),), -0.4, 0.0), -1.0, 1.0)
    out_weight = bell_draw_with(key_of[5], (D, D_OUT), D ** -0.5, 0.1875, ((0, 8), (1, 64)), (0, 1, 64, 4.0))
    return {"features": features, "short_weight": short_weight, "decay_rate": decay_rate, "residue": residue, "skip_gain": skip_gain, "out_weight": out_weight}


def reference(features, short_weight, decay_rate, residue, skip_gain, out_weight):
    hi = lax.Precision.HIGHEST
    xs = features.astype(jnp.float32)
    conv = jnp.zeros(xs.shape, jnp.float32)
    for j in range(KS):
        moved = jnp.pad(xs, ((0, 0), (j, 0), (0, 0)))[:, :SEQ, :]
        conv = conv + short_weight[:, j][:, None, :] * moved
    q_lane = conv[0]
    gated = (conv[1] * conv[2]).astype(jnp.bfloat16)
    coef = residue * jnp.sqrt(-jnp.expm1(-2.0 * decay_rate))
    lags = jnp.arange(TOK_DEV, dtype=jnp.float32)
    near_filter = lax.optimization_barrier(jnp.sum(coef[:, :, None] * jnp.exp(-decay_rate[:, :, None] * lags[None, None, :]), axis=1)).astype(jnp.bfloat16)
    rows = jnp.arange(TOK_DEV, dtype=jnp.int32)
    offset = rows[:, None] - rows[None, :]
    toeplitz = jnp.where(offset[None] >= 0, near_filter[:, jnp.clip(offset, 0, TOK_DEV - 1)], jnp.zeros((), jnp.bfloat16)).astype(jnp.float32)
    far_basis = coef[None] * jnp.exp(-decay_rate[None] * (lags + 1.0)[:, None, None])
    end_basis = jnp.exp(-decay_rate[None] * (TOK_DEV - 1.0 - lags)[:, None, None])
    block_decay = jnp.exp(-decay_rate * TOK_DEV)
    width = D // G
    blocks = gated.astype(jnp.float32).reshape(SEQ // TOK_DEV, TOK_DEV, G, width)

    def step(state, block):
        near = jnp.einsum('gts,sgw->tgw', toeplitz, block, precision=hi)
        far = jnp.einsum('tgs,gws->tgw', far_basis, state, precision=hi)
        state = block_decay[:, None, :] * state + jnp.einsum('tgs,tgw->gws', end_basis, block, precision=hi)
        return (state, near + far)
    start = jnp.zeros((G, width, S), jnp.float32)
    _, outs = lax.scan(step, start, blocks)
    filtered = outs.reshape(SEQ, D) + skip_gain[None, :] * gated.astype(jnp.float32)
    mixed = (q_lane * filtered).astype(jnp.bfloat16)
    return jnp.dot(mixed, out_weight, preferred_element_type=jnp.float32).astype(jnp.bfloat16)
```

```python
import jax
import jax.numpy as jnp
import numpy as np
from jax import lax
from jax.sharding import Mesh
from jax.sharding import PartitionSpec as P

CTX = ("chi", "clo")


def shifted(value, axis, count, by):
    pairs = [(i, i + by) for i in range(count) if i + by < count]
    return lax.ppermute(value, axis, pairs)


def make_per_device(n_ctx, n_tp):
    n_lo = n_ctx // n_tp

    def per_device(features, short_weight, decay_rate, residue, skip_gain, out_weight):
        rows = features.shape[1]
        chans = features.shape[2]
        groups = decay_rate.shape[0]
        modes = decay_rate.shape[1]
        width = chans // groups
        taps = short_weight.shape[1]

        rim = shifted(features[:, rows - (taps - 1) :, :], CTX, n_ctx, 1)
        extended = jnp.concatenate([rim, features], axis=1)
        conv = jnp.zeros(features.shape, jnp.float32)
        for j in range(taps):
            conv = conv + short_weight[:, j][:, None, :] * extended[
                :, taps - 1 - j : taps - 1 - j + rows, :
            ].astype(jnp.float32)
        q_lane = conv[0]
        gated = (conv[1] * conv[2]).astype(jnp.bfloat16)
        gated_wide = gated.astype(jnp.float32)

        coef = residue * jnp.sqrt(-jnp.expm1(-2.0 * decay_rate))
        lags = jnp.arange(rows, dtype=jnp.float32)
        near_filter = jnp.sum(
            coef[:, :, None] * jnp.exp(-decay_rate[:, :, None] * lags[None, None, :]), axis=1
        ).astype(jnp.bfloat16)

        index = np.arange(rows)
        onehot = (
            (index[None, :, None] - index[None, None, :]) == index[:, None, None]
        ).astype(np.float32)
        onehot = jnp.asarray(onehot.reshape(rows, rows * rows), jnp.bfloat16)
        toeplitz = jnp.dot(near_filter, onehot, preferred_element_type=jnp.float32)
        toeplitz = toeplitz.astype(jnp.bfloat16).reshape(groups, rows, rows)
        near = jnp.einsum(
            "gts,sgw->tgw",
            toeplitz,
            gated.reshape(rows, groups, width),
            preferred_element_type=jnp.float32,
        ).reshape(rows, chans)

        rate_c = jnp.repeat(decay_rate.T, width, axis=1)
        coef_c = jnp.repeat(coef.T, width, axis=1)
        end_basis = jnp.exp(-rate_c[None] * (rows - 1.0 - lags)[:, None, None])
        own_state = jnp.sum(end_basis * gated_wide[:, None, :], axis=0)
        state = shifted(own_state, CTX, n_ctx, 1)
        by = 1
        while by < n_ctx:
            decay = jnp.exp(-rate_c * float(rows * by))
            state = state + decay * shifted(state, CTX, n_ctx, by)
            by *= 2
        far_basis = coef_c[None] * jnp.exp(-rate_c[None] * (lags + 1.0)[:, None, None])
        far = jnp.sum(far_basis * state[None], axis=1)

        mixed = (q_lane * (near + far + skip_gain[None, :] * gated_wide)).astype(jnp.bfloat16)

        tokens = lax.all_gather(mixed, "chi", axis=0)
        weight = lax.all_gather(out_weight, "clo", axis=1, tiled=True)
        partial = jnp.einsum(
            "ktc,co->kto", tokens, weight, preferred_element_type=jnp.float32
        )
        block = lax.psum_scatter(partial, "tp", scatter_dimension=0, tiled=False)
        block = block.astype(jnp.bfloat16)
        swap = [(a * n_tp + b, b * n_tp + a) for a in range(n_tp) for b in range(n_tp)]
        return lax.ppermute(block, ("chi", "tp"), swap)

    return per_device


def solution(mesh):
    n_ctx = mesh.shape["ctx"]
    n_tp = mesh.shape["tp"]
    devices = np.asarray(mesh.devices).reshape(n_tp, n_ctx // n_tp, n_tp)
    split = Mesh(devices, ("chi", "clo", "tp"))
    placed = (
        P(None, CTX, "tp"),
        P(None, None, "tp"),
        P("tp", None),
        P("tp", None),
        P("tp"),
        P("tp", CTX),
    )
    return jax.shard_map(
        make_per_device(n_ctx, n_tp),
        mesh=split,
        in_specs=placed,
        out_specs=P(CTX, "tp"),
        check_vma=False,
    )
```

```python
import jax
import jax.numpy as jnp
import numpy as np
from jax import lax
from jax.sharding import Mesh
from jax.sharding import PartitionSpec as P

CTX = ("chi", "clo")


def shifted(value, axis, count, by):
    pairs = [(i, i + by) for i in range(count) if i + by < count]
    return lax.ppermute(value, axis, pairs)


def rotated(value, axis, count, by):
    return lax.ppermute(value, axis, [(i, (i + by) % count) for i in range(count)])


def digit_rotated(value, count, stride, size, by):
    pairs = []
    for i in range(count):
        d = (i // stride) % size
        pairs.append((i, i + (((d + by) % size) - d) * stride))
    return lax.ppermute(value, CTX, pairs)


def scan_levels(count):
    levels = []
    while count > 1:
        size = 4 if count % 4 == 0 else count
        levels.append(size)
        count //= size
    return levels


def make_per_device(n_ctx, n_tp):
    n_lo = n_ctx // n_tp

    def per_device(features, short_weight, decay_rate, residue, skip_gain, out_weight):
        rows = features.shape[1]
        chans = features.shape[2]
        groups = decay_rate.shape[0]
        width = chans // groups
        taps = short_weight.shape[1]
        chi = lax.axis_index("chi")
        clo = lax.axis_index("clo")
        me = chi * n_lo + clo
        tp = lax.axis_index("tp")

        weight = lax.all_gather(out_weight, "chi", axis=1, tiled=True)
        weight = weight.reshape(chans, n_tp, -1)

        rim = shifted(features[:, rows - (taps - 1) :, :], CTX, n_ctx, 1)
        extended = jnp.concatenate([rim, features], axis=1)
        conv = jnp.zeros(features.shape, jnp.float32)
        for j in range(taps):
            conv = conv + short_weight[:, j][:, None, :] * extended[
                :, taps - 1 - j : taps - 1 - j + rows, :
            ].astype(jnp.float32)
        q_lane = conv[0]
        gated = (conv[1] * conv[2]).astype(jnp.bfloat16)
        gated_wide = gated.astype(jnp.float32)

        coef = residue * jnp.sqrt(-jnp.expm1(-2.0 * decay_rate))
        lags = jnp.arange(rows, dtype=jnp.float32)
        near_filter = jnp.sum(
            coef[:, :, None] * jnp.exp(-decay_rate[:, :, None] * lags[None, None, :]), axis=1
        ).astype(jnp.bfloat16)

        index = np.arange(rows)
        onehot = (
            (index[None, :, None] - index[None, None, :]) == index[:, None, None]
        ).astype(np.float32)
        onehot = jnp.asarray(onehot.reshape(rows, rows * rows), jnp.bfloat16)
        toeplitz = jnp.dot(near_filter, onehot, preferred_element_type=jnp.float32)
        toeplitz = toeplitz.astype(jnp.bfloat16).reshape(groups, rows, rows)
        near = jnp.einsum(
            "gts,sgw->tgw",
            toeplitz,
            gated.reshape(rows, groups, width),
            preferred_element_type=jnp.float32,
        ).reshape(rows, chans)

        rate_c = jnp.repeat(decay_rate.T, width, axis=1)
        coef_c = jnp.repeat(coef.T, width, axis=1)

        def decay(blocks):
            return jnp.exp(-rate_c * (rows * blocks.astype(jnp.float32)))

        end_basis = jnp.exp(-rate_c[None] * (rows - 1.0 - lags)[:, None, None])
        own_state = jnp.sum(end_basis * gated_wide[:, None, :], axis=0)
        before = jnp.zeros_like(own_state)
        total = own_state
        stride = 1
        for size in scan_levels(n_ctx):
            d = (me // stride) % size
            r = me % stride
            merged = decay((size - 1 - d) * stride) * total
            for by in range(1, size):
                got = digit_rotated(total, n_ctx, stride, size, by)
                src = (d - by) % size
                before = before + jnp.where(
                    by <= d, decay((by - 1) * stride + r) * got, jnp.zeros_like(got)
                )
                merged = merged + decay((size - 1 - src) * stride) * got
            total = merged
            stride *= size
        far_basis = coef_c[None] * jnp.exp(-rate_c[None] * (lags + 1.0)[:, None, None])
        far = jnp.sum(far_basis * before[None], axis=1)

        mixed = (q_lane * (near + far + skip_gain[None, :] * gated_wide)).astype(jnp.bfloat16)

        tokens = [mixed] + [rotated(mixed, "clo", n_lo, by) for by in range(1, n_lo)]
        tokens = jnp.stack(tokens)
        partial = jnp.einsum(
            "ktc,cqo->qkto", tokens, weight, preferred_element_type=jnp.float32
        )
        summed = lax.dynamic_index_in_dim(partial, tp, 0, keepdims=False)
        for by in range(1, n_tp):
            piece = lax.dynamic_index_in_dim(partial, (tp + by) % n_tp, 0, keepdims=False)
            summed = summed + rotated(piece, "tp", n_tp, by)
        summed = summed.astype(jnp.bfloat16)
        back = [summed[0]] + [
            rotated(summed[by], "clo", n_lo, n_lo - by) for by in range(1, n_lo)
        ]
        back = jnp.stack(back)
        back = jnp.roll(back, clo, axis=0)
        return back.transpose(1, 0, 2).reshape(rows, -1)

    return per_device


def solution(mesh):
    n_ctx = mesh.shape["ctx"]
    n_tp = mesh.shape["tp"]
    devices = np.asarray(mesh.devices).reshape(n_tp, n_ctx // n_tp, n_tp)
    split = Mesh(devices, ("chi", "clo", "tp"))
    placed = (
        P(None, CTX, "tp"),
        P(None, None, "tp"),
        P("tp", None),
        P("tp", None),
        P("tp"),
        P("tp", CTX),
    )
    return jax.shard_map(
        make_per_device(n_ctx, n_tp),
        mesh=split,
        in_specs=placed,
        out_specs=P(CTX, "tp"),
        check_vma=False,
    )
```

```python
import jax
import jax.numpy as jnp
import numpy as np
from jax import lax
from jax.sharding import Mesh
from jax.sharding import PartitionSpec as P

CTX = ("chi", "clo")


def shifted(value, axis, count, by):
    pairs = [(i, i + by) for i in range(count) if i + by < count]
    return lax.ppermute(value, axis, pairs)


def rotated(value, axis, count, by):
    return lax.ppermute(value, axis, [(i, (i + by) % count) for i in range(count)])


def digit_rotated(value, count, stride, size, by):
    pairs = []
    for i in range(count):
        d = (i // stride) % size
        pairs.append((i, i + (((d + by) % size) - d) * stride))
    return lax.ppermute(value, CTX, pairs)


def scan_levels(count):
    levels = []
    while count > 1:
        size = 4 if count % 4 == 0 else count
        levels.append(size)
        count //= size
    return levels


def make_per_device(n_ctx, n_tp):
    n_lo = n_ctx // n_tp

    def per_device(features, short_weight, decay_rate, residue, skip_gain, out_weight):
        rows = features.shape[1]
        chans = features.shape[2]
        groups = decay_rate.shape[0]
        width = chans // groups
        taps = short_weight.shape[1]
        chi = lax.axis_index("chi")
        clo = lax.axis_index("clo")
        me = chi * n_lo + clo
        tp = lax.axis_index("tp")

        weight = lax.all_gather(out_weight, "chi", axis=1, tiled=True)
        weight = weight.reshape(chans, n_tp, -1)

        rim = shifted(features[:, rows - (taps - 1) :, :], CTX, n_ctx, 1)
        extended = jnp.concatenate([rim, features], axis=1)
        conv = jnp.zeros(features.shape, jnp.float32)
        for j in range(taps):
            conv = conv + short_weight[:, j][:, None, :] * extended[
                :, taps - 1 - j : taps - 1 - j + rows, :
            ].astype(jnp.float32)
        q_lane = conv[0]
        gated = (conv[1] * conv[2]).astype(jnp.bfloat16)
        gated_wide = gated.astype(jnp.float32)

        coef = residue * jnp.sqrt(-jnp.expm1(-2.0 * decay_rate))
        lags = jnp.arange(rows, dtype=jnp.float32)
        near_filter = jnp.sum(
            coef[:, :, None] * jnp.exp(-decay_rate[:, :, None] * lags[None, None, :]), axis=1
        ).astype(jnp.bfloat16)

        index = np.arange(rows)
        onehot = (
            (index[None, :, None] - index[None, None, :]) == index[:, None, None]
        ).astype(np.float32)
        onehot = jnp.asarray(onehot.reshape(rows, rows * rows), jnp.bfloat16)
        toeplitz = jnp.dot(near_filter, onehot, preferred_element_type=jnp.float32)
        toeplitz = toeplitz.astype(jnp.bfloat16).reshape(groups, rows, rows)
        near = jnp.einsum(
            "gts,sgw->tgw",
            toeplitz,
            gated.reshape(rows, groups, width),
            preferred_element_type=jnp.float32,
        ).reshape(rows, chans)

        rate_c = jnp.repeat(decay_rate.T, width, axis=1)
        coef_c = jnp.repeat(coef.T, width, axis=1)

        def decay(blocks):
            return jnp.exp(-rate_c * (rows * blocks.astype(jnp.float32)))

        end_basis = jnp.exp(-rate_c[None] * (rows - 1.0 - lags)[:, None, None])
        own_state = jnp.sum(end_basis * gated_wide[:, None, :], axis=0)
        before = jnp.zeros_like(own_state)
        total = own_state
        stride = 1
        for size in scan_levels(n_ctx):
            d = (me // stride) % size
            r = me % stride
            merged = decay((size - 1 - d) * stride) * total
            for by in range(1, size):
                got = digit_rotated(total, n_ctx, stride, size, by)
                src = (d - by) % size
                before = before + jnp.where(
                    by <= d, decay((by - 1) * stride + r) * got, jnp.zeros_like(got)
                )
                merged = merged + decay((size - 1 - src) * stride) * got
            total = merged
            stride *= size
        far_basis = coef_c[None] * jnp.exp(-rate_c[None] * (lags + 1.0)[:, None, None])
        far = jnp.sum(far_basis * before[None], axis=1)

        mixed = (q_lane * (near + far + skip_gain[None, :] * gated_wide)).astype(jnp.bfloat16)

        spread = jnp.broadcast_to(mixed[None], (n_lo,) + mixed.shape)
        tokens = lax.all_to_all(spread, "clo", 0, 0, tiled=True)
        partial = jnp.einsum(
            "ktc,cqo->qkto", tokens, weight, preferred_element_type=jnp.float32
        )
        pieces = lax.all_to_all(partial, "tp", 0, 0, tiled=True)
        summed = jnp.sum(pieces, axis=0).astype(jnp.bfloat16)
        back = lax.all_to_all(summed, "clo", 0, 0, tiled=True)
        return back.transpose(1, 0, 2).reshape(rows, -1)

    return per_device


def solution(mesh):
    n_ctx = mesh.shape["ctx"]
    n_tp = mesh.shape["tp"]
    devices = np.asarray(mesh.devices).reshape(n_tp, n_ctx // n_tp, n_tp)
    split = Mesh(devices, ("chi", "clo", "tp"))
    placed = (
        P(None, CTX, "tp"),
        P(None, None, "tp"),
        P("tp", None),
        P("tp", None),
        P("tp"),
        P("tp", CTX),
    )
    return jax.shard_map(
        make_per_device(n_ctx, n_tp),
        mesh=split,
        in_specs=placed,
        out_specs=P(CTX, "tp"),
        check_vma=False,
    )
```

```python
import jax
import jax.numpy as jnp
import numpy as np
from jax import lax
from jax.sharding import Mesh
from jax.sharding import PartitionSpec as P


CTX = ("chi", "clo")


def shifted(value, axis, count, by):
    pairs = [(i, i + by) for i in range(count) if i + by < count]
    return lax.ppermute(value, axis, pairs)


def make_per_device(n_ctx, n_tp):
    n_lo = n_ctx // n_tp

    def per_device(features, short_weight, decay_rate, residue, skip_gain, out_weight):
        rows = features.shape[1]
        chans = features.shape[2]
        groups = decay_rate.shape[0]
        width = chans // groups
        taps = short_weight.shape[1]
        chi = lax.axis_index("chi")
        clo = lax.axis_index("clo")
        me = chi * n_lo + clo

        weight = lax.all_gather(out_weight, "clo", axis=1, tiled=True)

        rim = shifted(features[:, rows - (taps - 1) :, :], CTX, n_ctx, 1)
        extended = jnp.concatenate([rim, features], axis=1)
        conv = jnp.zeros(features.shape, jnp.float32)
        for j in range(taps):
            conv = conv + short_weight[:, j][:, None, :] * extended[
                :, taps - 1 - j : taps - 1 - j + rows, :
            ].astype(jnp.float32)
        q_lane = conv[0]
        gated = (conv[1] * conv[2]).astype(jnp.bfloat16)
        gated_wide = gated.astype(jnp.float32)

        coef = residue * jnp.sqrt(-jnp.expm1(-2.0 * decay_rate))
        lags = jnp.arange(rows, dtype=jnp.float32)
        near_filter = jnp.sum(
            coef[:, :, None] * jnp.exp(-decay_rate[:, :, None] * lags[None, None, :]), axis=1
        ).astype(jnp.bfloat16)

        index = np.arange(rows)
        onehot = (
            (index[None, :, None] - index[None, None, :]) == index[:, None, None]
        ).astype(np.float32)
        onehot = jnp.asarray(onehot.reshape(rows, rows * rows), jnp.bfloat16)
        toeplitz = jnp.dot(near_filter, onehot, preferred_element_type=jnp.float32)
        toeplitz = toeplitz.astype(jnp.bfloat16).reshape(groups, rows, rows)
        near = jnp.einsum(
            "gts,sgw->tgw",
            toeplitz,
            gated.reshape(rows, groups, width),
            preferred_element_type=jnp.float32,
        ).reshape(rows, chans)

        rate_c = jnp.repeat(decay_rate.T, width, axis=1)
        coef_c = jnp.repeat(coef.T, width, axis=1)

        def decay(blocks):
            return jnp.exp(-rate_c * (rows * blocks.astype(jnp.float32)))

        end_basis = jnp.exp(-rate_c[None] * (rows - 1.0 - lags)[:, None, None])
        own_state = jnp.sum(end_basis * gated_wide[:, None, :], axis=0)
        before = jnp.zeros_like(own_state)
        total = own_state
        stride = 1
        for axis, size, digit in (("clo", n_lo, clo), ("chi", n_tp, chi)):
            spread = jnp.broadcast_to(total[None], (size,) + total.shape)
            got = lax.all_to_all(spread, axis, 0, 0, tiled=True)
            src_digit = jnp.arange(size)
            gap = (digit - src_digit - 1) * stride + me % stride
            weight_in = jnp.where(
                (src_digit < digit)[:, None, None],
                decay(jnp.maximum(gap, 0)[:, None, None]),
                0.0,
            )
            before = before + jnp.sum(weight_in * got, axis=0)
            total = jnp.sum(decay(((size - 1 - src_digit) * stride)[:, None, None]) * got, axis=0)
            stride *= size
        far_basis = coef_c[None] * jnp.exp(-rate_c[None] * (lags + 1.0)[:, None, None])
        far = jnp.sum(far_basis * before[None], axis=1)

        mixed = (q_lane * (near + far + skip_gain[None, :] * gated_wide)).astype(jnp.bfloat16)

        spread = jnp.broadcast_to(mixed[None], (n_tp,) + mixed.shape)
        tokens = lax.all_to_all(spread, "chi", 0, 0, tiled=True)
        partial = jnp.einsum(
            "ktc,co->kto", tokens, weight, preferred_element_type=jnp.float32
        )
        pieces = lax.all_to_all(partial, "tp", 0, 0, tiled=True)
        block = jnp.sum(pieces, axis=0).astype(jnp.bfloat16)
        swap = [(a * n_tp + b, b * n_tp + a) for a in range(n_tp) for b in range(n_tp)]
        return lax.ppermute(block, ("chi", "tp"), swap)

    return per_device


def solution(mesh):
    n_ctx = mesh.shape["ctx"]
    n_tp = mesh.shape["tp"]
    devices = np.asarray(mesh.devices).reshape(n_tp, n_ctx // n_tp, n_tp)
    split = Mesh(devices, ("chi", "clo", "tp"))
    placed = (
        P(None, CTX, "tp"),
        P(None, None, "tp"),
        P("tp", None),
        P("tp", None),
        P("tp"),
        P("tp", CTX),
    )
    return jax.shard_map(
        make_per_device(n_ctx, n_tp),
        mesh=split,
        in_specs=placed,
        out_specs=P(CTX, "tp"),
        check_vma=False,
    )
```

```python
import jax
import jax.numpy as jnp
import numpy as np
from jax import lax
from jax.sharding import Mesh
from jax.sharding import PartitionSpec as P


CTX = ("chi", "clo")


def shifted(value, axis, count, by):
    pairs = [(i, i + by) for i in range(count) if i + by < count]
    return lax.ppermute(value, axis, pairs)


def make_per_device(n_ctx, n_tp):
    n_lo = n_ctx // n_tp

    def per_device(features, short_weight, decay_rate, residue, skip_gain, out_weight):
        rows = features.shape[1]
        chans = features.shape[2]
        groups = decay_rate.shape[0]
        width = chans // groups
        taps = short_weight.shape[1]
        clo = lax.axis_index("clo")

        weight = lax.all_gather(out_weight, "chi", axis=1, tiled=True)
        weight = weight.reshape(chans, n_tp, -1)

        rim = shifted(features[:, rows - (taps - 1) :, :], CTX, n_ctx, 1)
        extended = jnp.concatenate([rim, features], axis=1)
        conv = jnp.zeros(features.shape, jnp.float32)
        for j in range(taps):
            conv = conv + short_weight[:, j][:, None, :] * extended[
                :, taps - 1 - j : taps - 1 - j + rows, :
            ].astype(jnp.float32)
        q_lane = conv[0]
        gated = (conv[1] * conv[2]).astype(jnp.bfloat16)
        gated_wide = gated.astype(jnp.float32)

        coef = residue * jnp.sqrt(-jnp.expm1(-2.0 * decay_rate))
        lags = jnp.arange(rows, dtype=jnp.float32)
        near_filter = jnp.sum(
            coef[:, :, None] * jnp.exp(-decay_rate[:, :, None] * lags[None, None, :]), axis=1
        ).astype(jnp.bfloat16)

        index = np.arange(rows)
        onehot = (
            (index[None, :, None] - index[None, None, :]) == index[:, None, None]
        ).astype(np.float32)
        onehot = jnp.asarray(onehot.reshape(rows, rows * rows), jnp.bfloat16)
        toeplitz = jnp.dot(near_filter, onehot, preferred_element_type=jnp.float32)
        toeplitz = toeplitz.astype(jnp.bfloat16).reshape(groups, rows, rows)
        near = jnp.einsum(
            "gts,sgw->tgw",
            toeplitz,
            gated.reshape(rows, groups, width),
            preferred_element_type=jnp.float32,
        ).reshape(rows, chans)

        rate_c = jnp.repeat(decay_rate.T, width, axis=1)
        coef_c = jnp.repeat(coef.T, width, axis=1)

        def decay(blocks):
            return jnp.exp(-rate_c * (rows * jnp.asarray(blocks, jnp.float32)))

        end_basis = jnp.exp(-rate_c[None] * (rows - 1.0 - lags)[:, None, None])
        own_state = jnp.sum(end_basis * gated_wide[:, None, :], axis=0)

        spread = jnp.broadcast_to(own_state[None], (n_lo,) + own_state.shape)
        got = lax.all_to_all(spread, "clo", 0, 0, tiled=True)
        src = jnp.arange(n_lo)
        gap = jnp.maximum(clo - src - 1, 0)[:, None, None]
        inside = jnp.where((src < clo)[:, None, None], decay(gap), 0.0)
        before = jnp.sum(inside * got, axis=0)
        group_total = jnp.sum(decay((n_lo - 1 - src)[:, None, None]) * got, axis=0)
        carried = group_total
        earlier = jnp.zeros_like(group_total)
        by = 1
        while by < n_tp:
            came = shifted(carried, "chi", n_tp, by)
            earlier = earlier + decay(n_lo * (by - 1)) * came
            carried = carried + decay(n_lo * by) * came
            by *= 2
        before = before + decay(clo) * earlier

        far_basis = coef_c[None] * jnp.exp(-rate_c[None] * (lags + 1.0)[:, None, None])
        far = jnp.sum(far_basis * before[None], axis=1)

        mixed = (q_lane * (near + far + skip_gain[None, :] * gated_wide)).astype(jnp.bfloat16)

        spread = jnp.broadcast_to(mixed[None], (n_lo,) + mixed.shape)
        tokens = lax.all_to_all(spread, "clo", 0, 0, tiled=True)
        partial = jnp.einsum(
            "ktc,cqo->qkto", tokens, weight, preferred_element_type=jnp.float32
        )
        pieces = lax.all_to_all(partial, "tp", 0, 0, tiled=True)
        summed = jnp.sum(pieces, axis=0).astype(jnp.bfloat16)
        back = lax.all_to_all(summed, "clo", 0, 0, tiled=True)
        return back.transpose(1, 0, 2).reshape(rows, -1)

    return per_device


def solution(mesh):
    n_ctx = mesh.shape["ctx"]
    n_tp = mesh.shape["tp"]
    devices = np.asarray(mesh.devices).reshape(n_tp, n_ctx // n_tp, n_tp)
    split = Mesh(devices, ("chi", "clo", "tp"))
    placed = (
        P(None, CTX, "tp"),
        P(None, None, "tp"),
        P("tp", None),
        P("tp", None),
        P("tp"),
        P("tp", CTX),
    )
    return jax.shard_map(
        make_per_device(n_ctx, n_tp),
        mesh=split,
        in_specs=placed,
        out_specs=P(CTX, "tp"),
        check_vma=False,
    )
```

```python
import jax
import jax.numpy as jnp
import numpy as np
from jax import lax
from jax.sharding import Mesh
from jax.sharding import PartitionSpec as P


CTX = ("chi", "clo")


def shifted(value, axis, count, by):
    pairs = [(i, i + by) for i in range(count) if i + by < count]
    return lax.ppermute(value, axis, pairs)


def make_per_device(n_ctx, n_tp):
    n_lo = n_ctx // n_tp

    def per_device(features, short_weight, decay_rate, residue, skip_gain, out_weight):
        rows = features.shape[1]
        chans = features.shape[2]
        groups = decay_rate.shape[0]
        width = chans // groups
        taps = short_weight.shape[1]
        chi = lax.axis_index("chi")
        clo = lax.axis_index("clo")

        weight = lax.all_gather(out_weight, "chi", axis=1, tiled=True)
        weight = weight.reshape(chans, n_tp, -1)

        rim = shifted(features[:, rows - (taps - 1) :, :], CTX, n_ctx, 1)
        extended = jnp.concatenate([rim, features], axis=1)
        conv = jnp.zeros(features.shape, jnp.float32)
        for j in range(taps):
            conv = conv + short_weight[:, j][:, None, :] * extended[
                :, taps - 1 - j : taps - 1 - j + rows, :
            ].astype(jnp.float32)
        q_lane = conv[0]
        gated = (conv[1] * conv[2]).astype(jnp.bfloat16)
        gated_wide = gated.astype(jnp.float32)

        coef = residue * jnp.sqrt(-jnp.expm1(-2.0 * decay_rate))
        lags = jnp.arange(rows, dtype=jnp.float32)
        near_filter = jnp.sum(
            coef[:, :, None] * jnp.exp(-decay_rate[:, :, None] * lags[None, None, :]), axis=1
        ).astype(jnp.bfloat16)

        index = np.arange(rows)
        onehot = (
            (index[None, :, None] - index[None, None, :]) == index[:, None, None]
        ).astype(np.float32)
        onehot = jnp.asarray(onehot.reshape(rows, rows * rows), jnp.bfloat16)
        toeplitz = jnp.dot(near_filter, onehot, preferred_element_type=jnp.float32)
        toeplitz = toeplitz.astype(jnp.bfloat16).reshape(groups, rows, rows)
        near = jnp.einsum(
            "gts,sgw->tgw",
            toeplitz,
            gated.reshape(rows, groups, width),
            preferred_element_type=jnp.float32,
        ).reshape(rows, chans)

        rate_c = jnp.repeat(decay_rate.T, width, axis=1)
        coef_c = jnp.repeat(coef.T, width, axis=1)

        def decay(blocks):
            return jnp.exp(-rate_c * (rows * jnp.asarray(blocks, jnp.float32)))

        end_basis = jnp.exp(-rate_c[None] * (rows - 1.0 - lags)[:, None, None])
        own_state = jnp.sum(end_basis * gated_wide[:, None, :], axis=0)

        spread = jnp.broadcast_to(own_state[None], (n_lo,) + own_state.shape)
        got = lax.all_to_all(spread, "clo", 0, 0, tiled=True)
        src = jnp.arange(n_lo)
        gap = jnp.maximum(clo - src - 1, 0)[:, None, None]
        inside = jnp.where((src < clo)[:, None, None], decay(gap), 0.0)
        before = jnp.sum(inside * got, axis=0)
        group_total = jnp.sum(decay((n_lo - 1 - src)[:, None, None]) * got, axis=0)
        flip = [
            (c * n_lo + m, m * n_lo + c) for c in range(n_tp) for m in range(n_tp) if c != m
        ]
        turned = lax.ppermute(group_total, CTX, flip)
        turned = jnp.where(chi == clo, group_total, turned)
        spread = jnp.broadcast_to(turned[None], (n_lo,) + turned.shape)
        totals = lax.all_to_all(spread, "clo", 0, 0, tiled=True)[:n_tp]
        rows_before = jnp.arange(n_tp)
        lag = jnp.maximum(chi - rows_before - 1, 0)[:, None, None]
        outside = jnp.where((rows_before < chi)[:, None, None], decay(n_lo * lag), 0.0)
        before = before + decay(clo) * jnp.sum(outside * totals, axis=0)

        far_basis = coef_c[None] * jnp.exp(-rate_c[None] * (lags + 1.0)[:, None, None])
        far = jnp.sum(far_basis * before[None], axis=1)

        mixed = (q_lane * (near + far + skip_gain[None, :] * gated_wide)).astype(jnp.bfloat16)

        spread = jnp.broadcast_to(mixed[None], (n_lo,) + mixed.shape)
        tokens = lax.all_to_all(spread, "clo", 0, 0, tiled=True)
        partial = jnp.einsum(
            "ktc,cqo->qkto", tokens, weight, preferred_element_type=jnp.float32
        )
        partial = partial.transpose(1, 0, 2, 3).reshape((n_lo * n_tp,) + partial.shape[2:])
        pieces = lax.all_to_all(partial, ("clo", "tp"), 0, 0, tiled=True)
        pieces = pieces.reshape((n_lo, n_tp) + pieces.shape[1:])
        summed = jnp.sum(pieces, axis=1).astype(jnp.bfloat16)
        return summed.transpose(1, 0, 2).reshape(rows, -1)

    return per_device


def solution(mesh):
    n_ctx = mesh.shape["ctx"]
    n_tp = mesh.shape["tp"]
    devices = np.asarray(mesh.devices).reshape(n_tp, n_ctx // n_tp, n_tp)
    split = Mesh(devices, ("chi", "clo", "tp"))
    placed = (
        P(None, CTX, "tp"),
        P(None, None, "tp"),
        P("tp", None),
        P("tp", None),
        P("tp"),
        P("tp", CTX),
    )
    return jax.shard_map(
        make_per_device(n_ctx, n_tp),
        mesh=split,
        in_specs=placed,
        out_specs=P(CTX, "tp"),
        check_vma=False,
    )
```

```python
import jax
import jax.numpy as jnp
import numpy as np
from jax import lax
from jax.sharding import Mesh
from jax.sharding import PartitionSpec as P


CTX = ("chi", "clo")
TP = ("x", "core")


def shifted(value, axis, count, by):
    pairs = [(i, i + by) for i in range(count) if i + by < count]
    return lax.ppermute(value, axis, pairs)


def make_per_device(n_ctx, n_tp):
    n_lo = n_ctx // n_tp
    n_x = n_tp // 2

    def per_device(features, short_weight, decay_rate, residue, skip_gain, out_weight):
        rows = features.shape[1]
        chans = features.shape[2]
        groups = decay_rate.shape[0]
        width = chans // groups
        taps = short_weight.shape[1]
        chi = lax.axis_index("chi")
        clo = lax.axis_index("clo")

        weight = lax.all_gather(out_weight, "chi", axis=1, tiled=True)
        weight = weight.reshape(chans, n_tp, -1)

        rim = shifted(features[:, rows - (taps - 1) :, :], CTX, n_ctx, 1)
        extended = jnp.concatenate([rim, features], axis=1)
        conv = jnp.zeros(features.shape, jnp.float32)
        for j in range(taps):
            conv = conv + short_weight[:, j][:, None, :] * extended[
                :, taps - 1 - j : taps - 1 - j + rows, :
            ].astype(jnp.float32)
        q_lane = conv[0]
        gated = (conv[1] * conv[2]).astype(jnp.bfloat16)
        gated_wide = gated.astype(jnp.float32)

        coef = residue * jnp.sqrt(-jnp.expm1(-2.0 * decay_rate))
        lags = jnp.arange(rows, dtype=jnp.float32)
        near_filter = jnp.sum(
            coef[:, :, None] * jnp.exp(-decay_rate[:, :, None] * lags[None, None, :]), axis=1
        ).astype(jnp.bfloat16)

        index = np.arange(rows)
        onehot = (
            (index[None, :, None] - index[None, None, :]) == index[:, None, None]
        ).astype(np.float32)
        onehot = jnp.asarray(onehot.reshape(rows, rows * rows), jnp.bfloat16)
        toeplitz = jnp.dot(near_filter, onehot, preferred_element_type=jnp.float32)
        toeplitz = toeplitz.astype(jnp.bfloat16).reshape(groups, rows, rows)
        near = jnp.einsum(
            "gts,sgw->tgw",
            toeplitz,
            gated.reshape(rows, groups, width),
            preferred_element_type=jnp.float32,
        ).reshape(rows, chans)

        rate_c = jnp.repeat(decay_rate.T, width, axis=1)
        coef_c = jnp.repeat(coef.T, width, axis=1)

        def decay(blocks):
            return jnp.exp(-rate_c * (rows * jnp.asarray(blocks, jnp.float32)))

        end_basis = jnp.exp(-rate_c[None] * (rows - 1.0 - lags)[:, None, None])
        own_state = jnp.sum(end_basis * gated_wide[:, None, :], axis=0)

        spread = jnp.broadcast_to(own_state[None], (n_lo,) + own_state.shape)
        got = lax.all_to_all(spread, "clo", 0, 0, tiled=True)
        src = jnp.arange(n_lo)
        gap = jnp.maximum(clo - src - 1, 0)[:, None, None]
        inside = jnp.where((src < clo)[:, None, None], decay(gap), 0.0)
        before = jnp.sum(inside * got, axis=0)
        group_total = jnp.sum(decay((n_lo - 1 - src)[:, None, None]) * got, axis=0)
        flip = [
            (c * n_lo + m, m * n_lo + c) for c in range(n_tp) for m in range(n_tp) if c != m
        ]
        turned = lax.ppermute(group_total, CTX, flip)
        turned = jnp.where(chi == clo, group_total, turned)
        spread = jnp.broadcast_to(turned[None], (n_lo,) + turned.shape)
        totals = lax.all_to_all(spread, "clo", 0, 0, tiled=True)[:n_tp]
        rows_before = jnp.arange(n_tp)
        lag = jnp.maximum(chi - rows_before - 1, 0)[:, None, None]
        outside = jnp.where((rows_before < chi)[:, None, None], decay(n_lo * lag), 0.0)
        before = before + decay(clo) * jnp.sum(outside * totals, axis=0)

        far_basis = coef_c[None] * jnp.exp(-rate_c[None] * (lags + 1.0)[:, None, None])
        far = jnp.sum(far_basis * before[None], axis=1)

        mixed = (q_lane * (near + far + skip_gain[None, :] * gated_wide)).astype(jnp.bfloat16)

        spread = jnp.broadcast_to(mixed[None], (n_lo,) + mixed.shape)
        tokens = lax.all_to_all(spread, "clo", 0, 0, tiled=True)
        partial = jnp.einsum(
            "ktc,cqo->kqto", tokens, weight, preferred_element_type=jnp.float32
        )
        partial = partial.reshape((n_lo, n_x, 2) + partial.shape[2:])
        core = lax.axis_index("core")
        mine = lax.dynamic_index_in_dim(partial, core, 2, keepdims=False)
        other = lax.dynamic_index_in_dim(partial, 1 - core, 2, keepdims=False)
        mine = mine + lax.ppermute(other, "core", [(0, 1), (1, 0)])
        mine = mine.reshape((n_lo * n_x,) + mine.shape[2:])
        pieces = lax.all_to_all(mine, ("clo", "x"), 0, 0, tiled=True)
        pieces = pieces.reshape((n_lo, n_x) + pieces.shape[1:])
        summed = jnp.sum(pieces, axis=1).astype(jnp.bfloat16)
        return summed.transpose(1, 0, 2).reshape(rows, -1)

    return per_device


def solution(mesh):
    n_ctx = mesh.shape["ctx"]
    n_tp = mesh.shape["tp"]
    devices = np.asarray(mesh.devices).reshape(n_tp, n_ctx // n_tp, n_tp // 2, 2)
    split = Mesh(devices, ("chi", "clo", "x", "core"))
    placed = (
        P(None, CTX, TP),
        P(None, None, TP),
        P(TP, None),
        P(TP, None),
        P(TP),
        P(TP, CTX),
    )
    return jax.shard_map(
        make_per_device(n_ctx, n_tp),
        mesh=split,
        in_specs=placed,
        out_specs=P(CTX, TP),
        check_vma=False,
    )
```

```python
import jax
import jax.numpy as jnp
import numpy as np
from jax import lax
from jax.sharding import Mesh
from jax.sharding import PartitionSpec as P


CTX = ("chi", "clo")
TP = ("x", "core")


def shifted(value, axis, count, by):
    pairs = [(i, i + by) for i in range(count) if i + by < count]
    return lax.ppermute(value, axis, pairs)


def make_per_device(n_ctx, n_tp):
    n_lo = n_ctx // n_tp
    n_x = n_tp // 2

    def per_device(features, short_weight, decay_rate, residue, skip_gain, out_weight):
        rows = features.shape[1]
        chans = features.shape[2]
        groups = decay_rate.shape[0]
        width = chans // groups
        taps = short_weight.shape[1]
        chi = lax.axis_index("chi")
        clo = lax.axis_index("clo")

        weight = lax.all_gather(out_weight, "chi", axis=1, tiled=True)
        weight = weight.reshape(chans, n_tp, -1)

        rim = shifted(features[:, rows - (taps - 1) :, :], CTX, n_ctx, 1)
        extended = jnp.concatenate([rim, features], axis=1)
        conv = jnp.zeros(features.shape, jnp.float32)
        for j in range(taps):
            conv = conv + short_weight[:, j][:, None, :] * extended[
                :, taps - 1 - j : taps - 1 - j + rows, :
            ].astype(jnp.float32)
        q_lane = conv[0]
        gated = (conv[1] * conv[2]).astype(jnp.bfloat16)
        gated_wide = gated.astype(jnp.float32)

        coef = residue * jnp.sqrt(-jnp.expm1(-2.0 * decay_rate))
        lags = jnp.arange(rows, dtype=jnp.float32)
        near_filter = jnp.sum(
            coef[:, :, None] * jnp.exp(-decay_rate[:, :, None] * lags[None, None, :]), axis=1
        ).astype(jnp.bfloat16)

        index = np.arange(rows)
        onehot = (
            (index[None, :, None] - index[None, None, :]) == index[:, None, None]
        ).astype(np.float32)
        onehot = jnp.asarray(onehot.reshape(rows, rows * rows), jnp.bfloat16)
        toeplitz = jnp.dot(near_filter, onehot, preferred_element_type=jnp.float32)
        toeplitz = toeplitz.astype(jnp.bfloat16).reshape(groups, rows, rows)
        near = jnp.einsum(
            "gts,sgw->tgw",
            toeplitz,
            gated.reshape(rows, groups, width),
            preferred_element_type=jnp.float32,
        ).reshape(rows, chans)

        rate_c = jnp.repeat(decay_rate.T, width, axis=1)
        coef_c = jnp.repeat(coef.T, width, axis=1)

        def decay(blocks):
            return jnp.exp(-rate_c * (rows * jnp.asarray(blocks, jnp.float32)))

        end_basis = jnp.exp(-rate_c[None] * (rows - 1.0 - lags)[:, None, None])
        own_state = jnp.sum(end_basis * gated_wide[:, None, :], axis=0)

        spread = jnp.broadcast_to(own_state[None], (n_lo,) + own_state.shape)
        got = lax.all_to_all(spread, "clo", 0, 0, tiled=True)
        src = jnp.arange(n_lo)
        gap = jnp.maximum(clo - src - 1, 0)[:, None, None]
        inside = jnp.where((src < clo)[:, None, None], decay(gap), 0.0)
        before = jnp.sum(inside * got, axis=0)
        group_total = jnp.sum(decay((n_lo - 1 - src)[:, None, None]) * got, axis=0)
        down = [
            (c * n_lo + b, ((c - b) % n_tp) * n_lo + b)
            for c in range(n_tp)
            for b in range(1, n_tp)
        ]
        turned = lax.ppermute(group_total, CTX, down)
        turned = jnp.where(clo == 0, group_total, turned)
        spread = jnp.broadcast_to(turned[None], (n_lo,) + turned.shape)
        totals = lax.all_to_all(spread, "clo", 0, 0, tiled=True)[:n_tp]
        totals = jnp.roll(totals, chi, axis=0)
        rows_before = jnp.arange(n_tp)
        lag = jnp.maximum(chi - rows_before - 1, 0)[:, None, None]
        outside = jnp.where((rows_before < chi)[:, None, None], decay(n_lo * lag), 0.0)
        before = before + decay(clo) * jnp.sum(outside * totals, axis=0)

        far_basis = coef_c[None] * jnp.exp(-rate_c[None] * (lags + 1.0)[:, None, None])
        far = jnp.sum(far_basis * before[None], axis=1)

        mixed = (q_lane * (near + far + skip_gain[None, :] * gated_wide)).astype(jnp.bfloat16)

        spread = jnp.broadcast_to(mixed[None], (n_lo,) + mixed.shape)
        tokens = lax.all_to_all(spread, "clo", 0, 0, tiled=True)
        partial = jnp.einsum(
            "ktc,cqo->kqto", tokens, weight, preferred_element_type=jnp.float32
        )
        partial = partial.reshape((n_lo, n_x, 2) + partial.shape[2:])
        core = lax.axis_index("core")
        mine = lax.dynamic_index_in_dim(partial, core, 2, keepdims=False)
        other = lax.dynamic_index_in_dim(partial, 1 - core, 2, keepdims=False)
        mine = mine + lax.ppermute(other, "core", [(0, 1), (1, 0)])
        mine = mine.reshape((n_lo * n_x,) + mine.shape[2:])
        pieces = lax.all_to_all(mine, ("clo", "x"), 0, 0, tiled=True)
        pieces = pieces.reshape((n_lo, n_x) + pieces.shape[1:])
        summed = jnp.sum(pieces, axis=1).astype(jnp.bfloat16)
        return summed.transpose(1, 0, 2).reshape(rows, -1)

    return per_device


def solution(mesh):
    n_ctx = mesh.shape["ctx"]
    n_tp = mesh.shape["tp"]
    devices = np.asarray(mesh.devices).reshape(n_tp, n_ctx // n_tp, n_tp // 2, 2)
    split = Mesh(devices, ("chi", "clo", "x", "core"))
    placed = (
        P(None, CTX, TP),
        P(None, None, TP),
        P(TP, None),
        P(TP, None),
        P(TP),
        P(TP, CTX),
    )
    return jax.shard_map(
        make_per_device(n_ctx, n_tp),
        mesh=split,
        in_specs=placed,
        out_specs=P(CTX, TP),
        check_vma=False,
    )
```

```python
import jax
import jax.numpy as jnp
import numpy as np
from jax import lax
from jax.sharding import Mesh
from jax.sharding import PartitionSpec as P


CTX = ("chi", "clo")
TP = ("x", "core")


def shifted(value, axis, count, by):
    pairs = [(i, i + by) for i in range(count) if i + by < count]
    return lax.ppermute(value, axis, pairs)


def make_per_device(n_ctx, n_tp):
    n_lo = n_ctx // n_tp
    n_x = n_tp // 2

    def per_device(features, short_weight, decay_rate, residue, skip_gain, out_weight):
        rows = features.shape[1]
        chans = features.shape[2]
        groups = decay_rate.shape[0]
        width = chans // groups
        taps = short_weight.shape[1]
        chi = lax.axis_index("chi")
        clo = lax.axis_index("clo")

        weight = lax.all_gather(out_weight, "chi", axis=1, tiled=True)
        weight = weight.reshape(chans, n_tp, -1)

        edge = taps - 1
        rim = shifted(features[:, rows - edge :, :], CTX, n_ctx, 1)

        def conv_of(extended, count):
            total = jnp.zeros((features.shape[0], count, chans), jnp.float32)
            for j in range(taps):
                total = total + short_weight[:, j][:, None, :] * extended[
                    :, edge - j : edge - j + count, :
                ].astype(jnp.float32)
            return total

        inner = conv_of(features, rows - edge)
        outer = conv_of(jnp.concatenate([rim, features[:, :edge, :]], axis=1), edge)
        conv = jnp.concatenate([outer, inner], axis=1)
        q_lane = conv[0]
        gated_inner = (inner[1] * inner[2]).astype(jnp.bfloat16)
        gated_outer = (outer[1] * outer[2]).astype(jnp.bfloat16)
        gated = jnp.concatenate([gated_outer, gated_inner], axis=0)
        gated_wide = gated.astype(jnp.float32)

        coef = residue * jnp.sqrt(-jnp.expm1(-2.0 * decay_rate))
        lags = jnp.arange(rows, dtype=jnp.float32)
        near_filter = jnp.sum(
            coef[:, :, None] * jnp.exp(-decay_rate[:, :, None] * lags[None, None, :]), axis=1
        ).astype(jnp.bfloat16)

        index = np.arange(rows)
        onehot = (
            (index[None, :, None] - index[None, None, :]) == index[:, None, None]
        ).astype(np.float32)
        onehot = jnp.asarray(onehot.reshape(rows, rows * rows), jnp.bfloat16)
        toeplitz = jnp.dot(near_filter, onehot, preferred_element_type=jnp.float32)
        toeplitz = toeplitz.astype(jnp.bfloat16).reshape(groups, rows, rows)
        near = jnp.einsum(
            "gts,sgw->tgw",
            toeplitz,
            gated.reshape(rows, groups, width),
            preferred_element_type=jnp.float32,
        ).reshape(rows, chans)

        rate_c = jnp.repeat(decay_rate.T, width, axis=1)
        coef_c = jnp.repeat(coef.T, width, axis=1)

        def decay(blocks):
            return jnp.exp(-rate_c * (rows * jnp.asarray(blocks, jnp.float32)))

        end_basis = jnp.exp(-rate_c[None] * (rows - 1.0 - lags)[:, None, None])
        own_state = jnp.sum(
            end_basis[edge:] * gated_inner.astype(jnp.float32)[:, None, :], axis=0
        ) + jnp.sum(end_basis[:edge] * gated_outer.astype(jnp.float32)[:, None, :], axis=0)

        spread = jnp.broadcast_to(own_state[None], (n_lo,) + own_state.shape)
        got = lax.all_to_all(spread, "clo", 0, 0, tiled=True)
        src = jnp.arange(n_lo)
        gap = jnp.maximum(clo - src - 1, 0)[:, None, None]
        inside = jnp.where((src < clo)[:, None, None], decay(gap), 0.0)
        before = jnp.sum(inside * got, axis=0)
        group_total = jnp.sum(decay((n_lo - 1 - src)[:, None, None]) * got, axis=0)
        flip = [
            (c * n_lo + m, m * n_lo + c) for c in range(n_tp) for m in range(n_tp) if c != m
        ]
        turned = lax.ppermute(group_total, CTX, flip)
        turned = jnp.where(chi == clo, group_total, turned)
        spread = jnp.broadcast_to(turned[None], (n_lo,) + turned.shape)
        totals = lax.all_to_all(spread, "clo", 0, 0, tiled=True)[:n_tp]
        rows_before = jnp.arange(n_tp)
        lag = jnp.maximum(chi - rows_before - 1, 0)[:, None, None]
        outside = jnp.where((rows_before < chi)[:, None, None], decay(n_lo * lag), 0.0)
        before = before + decay(clo) * jnp.sum(outside * totals, axis=0)

        far_basis = coef_c[None] * jnp.exp(-rate_c[None] * (lags + 1.0)[:, None, None])
        far = jnp.sum(far_basis * before[None], axis=1)

        mixed = (q_lane * (near + far + skip_gain[None, :] * gated_wide)).astype(jnp.bfloat16)

        spread = jnp.broadcast_to(mixed[None], (n_lo,) + mixed.shape)
        tokens = lax.all_to_all(spread, "clo", 0, 0, tiled=True)
        partial = jnp.einsum(
            "ktc,cqo->kqto", tokens, weight, preferred_element_type=jnp.float32
        )
        partial = partial.reshape((n_lo, n_x, 2) + partial.shape[2:])
        core = lax.axis_index("core")
        mine = lax.dynamic_index_in_dim(partial, core, 2, keepdims=False)
        other = lax.dynamic_index_in_dim(partial, 1 - core, 2, keepdims=False)
        mine = mine + lax.ppermute(other, "core", [(0, 1), (1, 0)])
        mine = mine.reshape((n_lo * n_x,) + mine.shape[2:])
        pieces = lax.all_to_all(mine, ("clo", "x"), 0, 0, tiled=True)
        pieces = pieces.reshape((n_lo, n_x) + pieces.shape[1:])
        summed = jnp.sum(pieces, axis=1).astype(jnp.bfloat16)
        return summed.transpose(1, 0, 2).reshape(rows, -1)

    return per_device


def solution(mesh):
    n_ctx = mesh.shape["ctx"]
    n_tp = mesh.shape["tp"]
    devices = np.asarray(mesh.devices).reshape(n_tp, n_ctx // n_tp, n_tp // 2, 2)
    split = Mesh(devices, ("chi", "clo", "x", "core"))
    placed = (
        P(None, CTX, TP),
        P(None, None, TP),
        P(TP, None),
        P(TP, None),
        P(TP),
        P(TP, CTX),
    )
    return jax.shard_map(
        make_per_device(n_ctx, n_tp),
        mesh=split,
        in_specs=placed,
        out_specs=P(CTX, TP),
        check_vma=False,
    )
```

```python
import jax
import jax.numpy as jnp
import numpy as np
from jax import lax
from jax.sharding import Mesh
from jax.sharding import PartitionSpec as P


CTX = ("chi", "clo")
TP = ("x", "core")


def shifted(value, axis, count, by):
    pairs = [(i, i + by) for i in range(count) if i + by < count]
    return lax.ppermute(value, axis, pairs)


def make_per_device(n_ctx, n_tp):
    n_lo = n_ctx // n_tp
    n_x = n_tp // 2

    def per_device(features, short_weight, decay_rate, residue, skip_gain, out_weight):
        rows = features.shape[1]
        chans = features.shape[2]
        groups = decay_rate.shape[0]
        width = chans // groups
        taps = short_weight.shape[1]
        chi = lax.axis_index("chi")
        clo = lax.axis_index("clo")

        weight = lax.all_gather(out_weight, "chi", axis=1, tiled=True)
        weight = weight.reshape(chans, n_tp, -1)

        rim = shifted(features[:, rows - (taps - 1) :, :], CTX, n_ctx, 1)
        extended = jnp.concatenate([rim, features], axis=1)
        conv = jnp.zeros(features.shape, jnp.float32)
        for j in range(taps):
            conv = conv + short_weight[:, j][:, None, :] * extended[
                :, taps - 1 - j : taps - 1 - j + rows, :
            ].astype(jnp.float32)
        q_lane = conv[0]
        gated = (conv[1] * conv[2]).astype(jnp.bfloat16)
        gated_wide = gated.astype(jnp.float32)

        coef = residue * jnp.sqrt(-jnp.expm1(-2.0 * decay_rate))
        lags = jnp.arange(rows, dtype=jnp.float32)
        near_filter = jnp.sum(
            coef[:, :, None] * jnp.exp(-decay_rate[:, :, None] * lags[None, None, :]), axis=1
        ).astype(jnp.bfloat16)

        index = np.arange(rows)
        onehot = (
            (index[None, :, None] - index[None, None, :]) == index[:, None, None]
        ).astype(np.float32)
        onehot = jnp.asarray(onehot.reshape(rows, rows * rows), jnp.bfloat16)
        toeplitz = jnp.dot(near_filter, onehot, preferred_element_type=jnp.float32)
        toeplitz = toeplitz.astype(jnp.bfloat16).reshape(groups, rows, rows)
        near = jnp.einsum(
            "gts,sgw->tgw",
            toeplitz,
            gated.reshape(rows, groups, width),
            preferred_element_type=jnp.float32,
        ).reshape(rows, chans)

        rate_c = jnp.repeat(decay_rate.T, width, axis=1)
        coef_c = jnp.repeat(coef.T, width, axis=1)

        def decay(blocks):
            return jnp.exp(-rate_c * (rows * jnp.asarray(blocks, jnp.float32)))

        end_basis = jnp.exp(-rate_c[None] * (rows - 1.0 - lags)[:, None, None])
        own_state = jnp.sum(end_basis * gated_wide[:, None, :], axis=0)

        spread = jnp.broadcast_to(own_state[None], (n_lo,) + own_state.shape)
        got = lax.all_to_all(spread, "clo", 0, 0, tiled=True)
        src = jnp.arange(n_lo)
        gap = jnp.maximum(clo - src - 1, 0)[:, None, None]
        inside = jnp.where((src < clo)[:, None, None], decay(gap), 0.0)
        before = jnp.sum(inside * got, axis=0)
        group_total = jnp.sum(decay((n_lo - 1 - src)[:, None, None]) * got, axis=0)
        flip = [
            (c * n_lo + m, m * n_lo + c) for c in range(n_tp) for m in range(n_tp) if c != m
        ]
        turned = lax.ppermute(group_total, CTX, flip)
        turned = jnp.where(chi == clo, group_total, turned)
        spread = jnp.broadcast_to(turned[None], (n_lo,) + turned.shape)
        totals = lax.all_to_all(spread, "clo", 0, 0, tiled=True)[:n_tp]
        rows_before = jnp.arange(n_tp)
        lag = jnp.maximum(chi - rows_before - 1, 0)[:, None, None]
        outside = jnp.where((rows_before < chi)[:, None, None], decay(n_lo * lag), 0.0)
        before = before + decay(clo) * jnp.sum(outside * totals, axis=0)

        far_basis = coef_c[None] * jnp.exp(-rate_c[None] * (lags + 1.0)[:, None, None])
        far = jnp.sum(far_basis * before[None], axis=1)

        mixed = (q_lane * (near + far + skip_gain[None, :] * gated_wide)).astype(jnp.bfloat16)

        spread = jnp.broadcast_to(mixed[None], (n_lo,) + mixed.shape)
        tokens = lax.all_to_all(spread, "clo", 0, 0, tiled=True)
        halves = weight.reshape(chans, n_x, 2, -1)
        core = lax.axis_index("core")
        w_mine = lax.dynamic_index_in_dim(halves, core, 2, keepdims=False)
        w_other = lax.dynamic_index_in_dim(halves, 1 - core, 2, keepdims=False)
        w_mine, w_other = lax.optimization_barrier((w_mine, w_other))
        other = jnp.einsum("ktc,cqo->kqto", tokens, w_other, preferred_element_type=jnp.float32)
        sent = lax.ppermute(other, "core", [(0, 1), (1, 0)])
        mine = jnp.einsum("ktc,cqo->kqto", tokens, w_mine, preferred_element_type=jnp.float32)
        mine = lax.optimization_barrier(mine) + sent
        mine = mine.reshape((n_lo * n_x,) + mine.shape[2:])
        pieces = lax.all_to_all(mine, ("clo", "x"), 0, 0, tiled=True)
        pieces = pieces.reshape((n_lo, n_x) + pieces.shape[1:])
        summed = jnp.sum(pieces, axis=1).astype(jnp.bfloat16)
        return summed.transpose(1, 0, 2).reshape(rows, -1)

    return per_device


def solution(mesh):
    n_ctx = mesh.shape["ctx"]
    n_tp = mesh.shape["tp"]
    devices = np.asarray(mesh.devices).reshape(n_tp, n_ctx // n_tp, n_tp // 2, 2)
    split = Mesh(devices, ("chi", "clo", "x", "core"))
    placed = (
        P(None, CTX, TP),
        P(None, None, TP),
        P(TP, None),
        P(TP, None),
        P(TP),
        P(TP, CTX),
    )
    return jax.shard_map(
        make_per_device(n_ctx, n_tp),
        mesh=split,
        in_specs=placed,
        out_specs=P(CTX, TP),
        check_vma=False,
    )
```

```python
import jax
import jax.numpy as jnp
import numpy as np
from jax import lax
from jax.sharding import Mesh
from jax.sharding import PartitionSpec as P


CTX = ("chi", "clo")
TP = ("x", "core")


def shifted(value, axis, count, by):
    pairs = [(i, i + by) for i in range(count) if i + by < count]
    return lax.ppermute(value, axis, pairs)


def make_per_device(n_ctx, n_tp):
    n_lo = n_ctx // n_tp
    n_x = n_tp // 2

    def per_device(features, short_weight, decay_rate, residue, skip_gain, out_weight):
        rows = features.shape[1]
        chans = features.shape[2]
        groups = decay_rate.shape[0]
        width = chans // groups
        taps = short_weight.shape[1]
        chi = lax.axis_index("chi")
        clo = lax.axis_index("clo")

        weight = lax.all_gather(out_weight, "chi", axis=1, tiled=True)
        weight = weight.reshape(chans, n_tp, -1)

        rim = shifted(features[:, rows - (taps - 1) :, :], CTX, n_ctx, 1)
        extended = jnp.concatenate([rim, features], axis=1)
        conv = jnp.zeros(features.shape, jnp.float32)
        for j in range(taps):
            conv = conv + short_weight[:, j][:, None, :] * extended[
                :, taps - 1 - j : taps - 1 - j + rows, :
            ].astype(jnp.float32)
        q_lane = conv[0]
        gated = (conv[1] * conv[2]).astype(jnp.bfloat16)
        gated_wide = gated.astype(jnp.float32)

        coef = residue * jnp.sqrt(-jnp.expm1(-2.0 * decay_rate))
        lags = jnp.arange(rows, dtype=jnp.float32)
        near_filter = jnp.sum(
            coef[:, :, None] * jnp.exp(-decay_rate[:, :, None] * lags[None, None, :]), axis=1
        ).astype(jnp.bfloat16)

        index = np.arange(rows)
        onehot = (
            (index[None, :, None] - index[None, None, :]) == index[:, None, None]
        ).astype(np.float32)
        onehot = jnp.asarray(onehot.reshape(rows, rows * rows), jnp.bfloat16)
        toeplitz = jnp.dot(near_filter, onehot, preferred_element_type=jnp.float32)
        toeplitz = toeplitz.astype(jnp.bfloat16).reshape(groups, rows, rows)
        near = jnp.einsum(
            "gts,sgw->tgw",
            toeplitz,
            gated.reshape(rows, groups, width),
            preferred_element_type=jnp.float32,
        ).reshape(rows, chans)

        rate_c = jnp.repeat(decay_rate.T, width, axis=1)
        coef_c = jnp.repeat(coef.T, width, axis=1)

        def decay(blocks):
            return jnp.exp(-rate_c * (rows * jnp.asarray(blocks, jnp.float32)))

        end_basis = jnp.exp(-rate_c[None] * (rows - 1.0 - lags)[:, None, None])
        own_state = jnp.sum(end_basis * gated_wide[:, None, :], axis=0)

        spread = jnp.broadcast_to(own_state[None], (n_lo,) + own_state.shape)
        got = lax.all_to_all(spread, "clo", 0, 0, tiled=True)
        src = jnp.arange(n_lo)
        gap = jnp.maximum(clo - src - 1, 0)[:, None, None]
        inside = jnp.where((src < clo)[:, None, None], decay(gap), 0.0)
        to_end = decay((n_lo - 1 - src)[:, None, None])
        rows_before = jnp.arange(n_tp)
        lag = jnp.maximum(chi - rows_before - 1, 0)[:, None, None]
        outside = jnp.where((rows_before < chi)[:, None, None], decay(n_lo * lag), 0.0)
        outside = outside * decay(clo)
        inside, to_end, outside = lax.optimization_barrier((inside, to_end, outside))
        before = jnp.sum(inside * got, axis=0)
        group_total = jnp.sum(to_end * got, axis=0)
        flip = [
            (c * n_lo + m, m * n_lo + c) for c in range(n_tp) for m in range(n_tp) if c != m
        ]
        turned = lax.ppermute(group_total, CTX, flip)
        turned = jnp.where(chi == clo, group_total, turned)
        spread = jnp.broadcast_to(turned[None], (n_lo,) + turned.shape)
        totals = lax.all_to_all(spread, "clo", 0, 0, tiled=True)[:n_tp]
        before = before + jnp.sum(outside * totals, axis=0)

        far_basis = coef_c[None] * jnp.exp(-rate_c[None] * (lags + 1.0)[:, None, None])
        far = jnp.sum(far_basis * before[None], axis=1)

        mixed = (q_lane * (near + far + skip_gain[None, :] * gated_wide)).astype(jnp.bfloat16)

        spread = jnp.broadcast_to(mixed[None], (n_lo,) + mixed.shape)
        tokens = lax.all_to_all(spread, "clo", 0, 0, tiled=True)
        halves = weight.reshape(chans, n_x, 2, -1)
        core = lax.axis_index("core")
        w_mine = lax.dynamic_index_in_dim(halves, core, 2, keepdims=False)
        w_other = lax.dynamic_index_in_dim(halves, 1 - core, 2, keepdims=False)
        w_mine, w_other = lax.optimization_barrier((w_mine, w_other))
        other = jnp.einsum("ktc,cqo->kqto", tokens, w_other, preferred_element_type=jnp.float32)
        sent = lax.ppermute(other, "core", [(0, 1), (1, 0)])
        mine = jnp.einsum("ktc,cqo->kqto", tokens, w_mine, preferred_element_type=jnp.float32)
        mine = lax.optimization_barrier(mine) + sent
        mine = mine.reshape((n_lo * n_x,) + mine.shape[2:])
        pieces = lax.all_to_all(mine, ("clo", "x"), 0, 0, tiled=True)
        pieces = pieces.reshape((n_lo, n_x) + pieces.shape[1:])
        summed = jnp.sum(pieces, axis=1).astype(jnp.bfloat16)
        return summed.transpose(1, 0, 2).reshape(rows, -1)

    return per_device


def solution(mesh):
    n_ctx = mesh.shape["ctx"]
    n_tp = mesh.shape["tp"]
    devices = np.asarray(mesh.devices).reshape(n_tp, n_ctx // n_tp, n_tp // 2, 2)
    split = Mesh(devices, ("chi", "clo", "x", "core"))
    placed = (
        P(None, CTX, TP),
        P(None, None, TP),
        P(TP, None),
        P(TP, None),
        P(TP),
        P(TP, CTX),
    )
    return jax.shard_map(
        make_per_device(n_ctx, n_tp),
        mesh=split,
        in_specs=placed,
        out_specs=P(CTX, TP),
        check_vma=False,
    )
```
